256 devices in a mesh: dp: 32 (over y_lo, z, core), expert: 8 (over y_hi, x).
Axes of the slice: x: 4, y: 4 (y_hi: 2, y_lo: 2; y = y_hi * 2 + y_lo), z: 8, core: 2. Of those that a mesh axis runs over, the one named last changes fastest.
Arguments:
- tokens: bfloat16 [65536, 2048], P(('dp', 'expert')), parts along dimension 0, may hold values from -6 to 6
- routes: int32 [65536, 2], P(('dp', 'expert')), parts along dimension 0, may hold values from 0 to 7, all different within a row; in each aligned block of 256 rows (0 to 255, 256 to 511, ...) at most 128 rows name the same one
- gate_values: bfloat16 [65536, 2], P(('dp', 'expert')), parts along dimension 0, may hold values from 0.099609375 to 1
- weight_in: bfloat16 [8, 2048, 1536], P('expert'), may hold values from -0.125 to 0.125
- weight_out: bfloat16 [8, 768, 2048], P('expert'), may hold values from -0.21875 to 0.21875
Outputs:
- mixed: bfloat16 [65536, 2048], P(('dp', 'expert')), parts along dimension 0
The draws below stay inside these ranges and needn't reach their ends.
There are 32 independent parts, one for each index of `dp`. The reference program is written for one: setup_inputs(seed, part) draws one part's arguments, and reference() takes and returns one part's arrays. A program takes and returns all parts, laid end to end along the dimension named above; an argument that names none is the same for every part. Nothing has to cross between parts.
Inputs may be any that keep to these rules, and one draw needn't show every extreme that they name: `routes`: each row names 2 different experts. In each aligned block of 256 rows (the rows of one device) no expert is named by more than 128 rows, a bound that some block reaches.
All inputs are finite; a program needn't handle non-finite values.
Results may differ from the reference program's by a relative error of at most 0.012.
Values may be sent and summed in bfloat16 or wider, within the bound.
No kernel may reach another device: no remote copies, remote signals or barrier semaphores. Data moves between devices by JAX's collectives and lax.ppermute only.
A program may use at most 128 MiB of HBM per device.

```python
import math
import jax
import jax.numpy as jnp
import numpy as np
from jax import lax

D = 2048
FF = 768
TOP = 2
TOK_DEV = 256
EXPERTS = 8
TOKENS = 2048
MOST_SRC = 128


def block_levels(rng, shape, pieces, least, largest):
    loudness = 1.0
    for axis_at, blocks in pieces:
        draws = jax.random.uniform(jax.random.fold_in(jax.random.fold_in(rng, 6), axis_at), (blocks,), jnp.float32, least / len(pieces), largest / len(pieces))
        loudness = loudness * jnp.repeat(jnp.exp(draws), shape[axis_at] // blocks).reshape((-1,) + (1,) * (len(shape) - 1 - axis_at))
    return loudness


def shared_out(own_key, own, number, rows, count, top, reach, slope):
    sequence = jax.random.permutation(own_key, count)
    heavy_load, usual = portions_of(count, rows * top, reach, slope, True), portions_of(count, rows * top, reach, slope, False)
    places = jnp.arange(count)

    def named(tallies, offset_by):
        used = int((tallies > 0).sum())
        fixed = max(1, used // 4)
        shifted = fixed + (places - fixed + offset_by * (used - fixed)) % max(1, count - fixed)
        return jnp.zeros((count,), jnp.int32).at[sequence[jnp.where(places < fixed, places, shifted)]].set(jnp.asarray(tallies, jnp.int32))

    tallies = jnp.where(number % 4 == 0, named(heavy_load, number // 4), named(usual, number - number // 4 - 1))
    mixed = jax.random.permutation(jax.random.fold_in(own, 3), count)
    donor, taker = mixed[0:count // 2 * 2:2], mixed[1:count // 2 * 2:2]
    slack = jnp.minimum(tallies[donor] - 1, reach - tallies[taker]) // 2
    slack = jnp.where((donor == sequence[0]) | (taker == sequence[0]) | (tallies[taker] == 0), 0, jnp.maximum(slack, 0))
    shifted = jax.random.randint(jax.random.fold_in(own, 4), (count // 2,), 0, 1 << 20) % (slack + 1)
    tallies = tallies.at[donor].add(-shifted).at[taker].add(shifted)
    items = jnp.searchsorted(jnp.cumsum(tallies), jnp.arange(rows * top), side="right").astype(jnp.int32)
    grid = items.reshape(top, rows).T
    grid = grid[jax.random.permutation(jax.random.fold_in(own, 1), rows)]
    offset_by = jax.random.randint(jax.random.fold_in(own, 2), (rows, 1), 0, top)
    return jnp.take_along_axis(grid, (jnp.arange(top)[None, :] + offset_by) % top, axis=1)


def portions_of(number_of, total, limit, skew, full):
    weights = [(1 << 20) // math.isqrt(grade ** skew) + 1 for grade in range(1, number_of + 1)]
    largest = limit if full else min(limit, max(-(-total // number_of), total * weights[0] // sum(weights)))
    least = 1 if total - largest >= number_of - 1 else 0
    given, spare = [largest] + [least] * (number_of - 1), total - largest - least * (number_of - 1)
    while spare > 0:
        free = [i for i in range(1, number_of) if given[i] < largest] or [i for i in range(1, number_of) if given[i] < limit]
        whole, remaining = sum([weights[i] for i in free]), spare
        for i in free:
            addition = min(limit - given[i], max(1, remaining * weights[i] // whole), spare)
            given[i] = given[i] + addition
            spare = spare - addition
    return np.array(given)


def scatter_about(rng, extent, spread, most, shards=(), kind=jnp.bfloat16):
    result = spread * jax.random.normal(rng, extent, jnp.float32)
    if shards:
        result = result * block_levels(rng, extent, shards, -0.22, 0.18)
    return jnp.clip(result, -most, most).astype(kind)


def setup_inputs(seed: int = 0, part: int = 0) -> dict:
    streams_of = jax.random.split(jax.random.key(seed), 6)
    part_splits = jax.random.split(jax.random.fold_in(streams_of[5], part), 6)
    tokens = scatter_about(part_splits[0], (TOKENS, D), 1.0, 6.0, ((0, 8),))
    routes_keys = jax.random.split(jax.random.fold_in(part_splits[1], 1), TOKENS // TOK_DEV)
    routes_turns = jax.random.permutation(jax.random.fold_in(part_splits[1], 3), TOKENS // TOK_DEV)
    routes = jax.vmap(lambda own, number: shared_out(jax.random.fold_in(part_splits[1], 2), own, number, TOK_DEV, EXPERTS, TOP, MOST_SRC, 1))(routes_keys, routes_turns).reshape((TOKENS, TOP))
    gate_values = jnp.clip(0.099609375 + 0.9003906 * jax.random.uniform(part_splits[2], (TOKENS, TOP), jnp.float32) ** block_levels(part_splits[2], (TOKENS, TOP), ((0, 8),), -0.2, 0.2), 0.099609375, 1.0).astype(jnp.bfloat16)
    weight_in = scatter_about(streams_of[3], (EXPERTS, D, 2 * FF), D ** -0.5, 0.125, ((0, 8),))
    weight_out = scatter_about(streams_of[4], (EXPERTS, FF, D), FF ** -0.5, 0.21875, ((0, 8),))
    return dict(tokens=tokens, routes=routes, gate_values=gate_values, weight_in=weight_in, weight_out=weight_out)


def reference(tokens, routes, gate_values, weight_in, weight_out):
    gates_wide = gate_values.astype(jnp.float32)

    def one_expert(summed, items):
        w_first, w_second, expert_id = items
        combine = jnp.sum(jnp.where(routes == expert_id, gates_wide, 0.0), axis=1)
        projected = jnp.dot(tokens, w_first, preferred_element_type=jnp.float32)
        hidden = (jax.nn.silu(projected[:, :FF]) * projected[:, FF:]).astype(jnp.bfloat16)
        expert_out = jnp.dot(hidden, w_second, preferred_element_type=jnp.float32)
        contribution = (expert_out * combine[:, None]).astype(jnp.bfloat16)
        return summed + contribution.astype(jnp.float32), None

    start = jnp.zeros((TOKENS, D), jnp.float32)
    summed, unused = lax.scan(one_expert, start, (weight_in, weight_out, jnp.arange(EXPERTS, dtype=jnp.int32)))
    return summed.astype(jnp.bfloat16)
```

```python
import jax
import jax.numpy as jnp
from jax import lax
from jax.sharding import PartitionSpec as P


def slot_matrix(routes, gate_values, groups, capacity):
    tok_rows = routes.shape[0]
    experts = jnp.arange(groups, dtype=jnp.int32)
    matched = routes[:, :, None] == experts[None, None, :]
    named = jnp.any(matched, axis=1)
    weight = jnp.sum(jnp.where(matched, gate_values.astype(jnp.float32)[:, :, None], 0.0), axis=1)
    position = jnp.cumsum(named.astype(jnp.int32), axis=0) - 1
    slots = jnp.arange(capacity, dtype=jnp.int32)
    picks = named.T[:, None, :] & (position.T[:, None, :] == slots[None, :, None])
    return picks.astype(jnp.bfloat16), weight.astype(jnp.bfloat16)


def local(tokens, routes, gate_values, weight_in, weight_out):
    groups = lax.axis_size("expert")
    tok_rows, width = tokens.shape
    capacity = min(tok_rows, 2 * tok_rows * routes.shape[1] // groups)
    hidden_units = weight_out.shape[1]
    me = lax.axis_index("expert")
    picks, weight = slot_matrix(routes, gate_values, groups, capacity)
    lanes = 128
    extended = jnp.concatenate(
        [tokens, jnp.pad(weight, ((0, 0), (0, lanes - groups)))], axis=1
    )
    outgoing = jnp.einsum(
        "ect,td->ecd", picks, extended, preferred_element_type=jnp.float32
    ).astype(jnp.bfloat16)
    incoming = lax.all_to_all(outgoing, "expert", 0, 0, tiled=True)
    rows = incoming[:, :, :width].reshape(groups * capacity, width)
    own = jnp.arange(groups, dtype=jnp.int32) == me
    gate = jnp.sum(
        jnp.where(own, incoming[:, :, width:width + groups].astype(jnp.float32), 0.0),
        axis=-1,
    ).reshape(-1, 1)
    projected = jnp.dot(rows, weight_in[0], preferred_element_type=jnp.float32)
    hidden = (jax.nn.silu(projected[:, :hidden_units]) * projected[:, hidden_units:]).astype(
        jnp.bfloat16
    )
    expert_out = jnp.dot(hidden, weight_out[0], preferred_element_type=jnp.float32)
    contribution = (expert_out * gate).astype(jnp.bfloat16).reshape(groups, capacity, width)
    returned = lax.all_to_all(contribution, "expert", 0, 0, tiled=True)
    mixed = jnp.einsum(
        "ect,ecd->td", picks, returned, preferred_element_type=jnp.float32
    )
    return mixed.astype(jnp.bfloat16)


def solution(mesh):
    in_specs = (
        P(("dp", "expert"), None),
        P(("dp", "expert"), None),
        P(("dp", "expert"), None),
        P("expert", None, None),
        P("expert", None, None),
    )
    out_specs = P(("dp", "expert"), None)
    return jax.shard_map(local, mesh=mesh, in_specs=in_specs, out_specs=out_specs, check_vma=False)
```

```python
import jax
import jax.numpy as jnp
from jax import lax
from jax.sharding import PartitionSpec as P


def slot_matrices(routes, gate_values, groups, capacity):
    experts = jnp.arange(groups, dtype=jnp.int32)
    matched = routes[:, :, None] == experts[None, None, :]
    named = jnp.any(matched, axis=1)
    weight = jnp.sum(jnp.where(matched, gate_values.astype(jnp.float32)[:, :, None], 0.0), axis=1)
    position = jnp.cumsum(named.astype(jnp.int32), axis=0) - 1
    slots = jnp.arange(capacity, dtype=jnp.int32)
    picks = named.T[:, None, :] & (position.T[:, None, :] == slots[None, :, None])
    weighted = jnp.where(picks, weight.T[:, None, :], 0.0)
    return picks.astype(jnp.bfloat16), weighted.astype(jnp.bfloat16)


def local(tokens, routes, gate_values, weight_in, weight_out):
    groups = lax.axis_size("expert")
    tok_rows, width = tokens.shape
    capacity = min(tok_rows, 2 * tok_rows * routes.shape[1] // groups)
    hidden_units = weight_out.shape[1]
    picks, weighted = slot_matrices(routes, gate_values, groups, capacity)
    outgoing = jnp.einsum(
        "ect,td->ecd", picks, tokens, preferred_element_type=jnp.float32
    ).astype(jnp.bfloat16)
    incoming = lax.all_to_all(outgoing, "expert", 0, 0, tiled=True)
    rows = incoming.reshape(groups * capacity, width)
    projected = jnp.dot(rows, weight_in[0], preferred_element_type=jnp.float32)
    hidden = (jax.nn.silu(projected[:, :hidden_units]) * projected[:, hidden_units:]).astype(
        jnp.bfloat16
    )
    expert_out = jnp.dot(hidden, weight_out[0], preferred_element_type=jnp.float32)
    expert_out = expert_out.astype(jnp.bfloat16).reshape(groups, capacity, width)
    returned = lax.all_to_all(expert_out, "expert", 0, 0, tiled=True)
    mixed = jnp.einsum(
        "ect,ecd->td", weighted, returned, preferred_element_type=jnp.float32
    )
    return mixed.astype(jnp.bfloat16)


def solution(mesh):
    in_specs = (
        P(("dp", "expert"), None),
        P(("dp", "expert"), None),
        P(("dp", "expert"), None),
        P("expert", None, None),
        P("expert", None, None),
    )
    out_specs = P(("dp", "expert"), None)
    return jax.shard_map(local, mesh=mesh, in_specs=in_specs, out_specs=out_specs, check_vma=False)
```

```python
import jax
import jax.numpy as jnp
from jax import lax
from jax.sharding import PartitionSpec as P

CHUNKS = 2


def slot_matrices(routes, gate_values, groups, capacity):
    experts = jnp.arange(groups, dtype=jnp.int32)
    matched = routes[:, :, None] == experts[None, None, :]
    named = jnp.any(matched, axis=1)
    weight = jnp.sum(jnp.where(matched, gate_values.astype(jnp.float32)[:, :, None], 0.0), axis=1)
    position = jnp.cumsum(named.astype(jnp.int32), axis=0) - 1
    slots = jnp.arange(capacity, dtype=jnp.int32)
    picks = named.T[:, None, :] & (position.T[:, None, :] == slots[None, :, None])
    weighted = jnp.where(picks, weight.T[:, None, :], 0.0)
    return picks.astype(jnp.bfloat16), weighted.astype(jnp.bfloat16)


def expert_rows(rows, w_first, w_second):
    hidden_units = w_second.shape[0]
    projected = jnp.dot(rows, w_first, preferred_element_type=jnp.float32)
    hidden = (jax.nn.silu(projected[:, :hidden_units]) * projected[:, hidden_units:]).astype(
        jnp.bfloat16
    )
    return jnp.dot(hidden, w_second, preferred_element_type=jnp.float32).astype(jnp.bfloat16)


def local(tokens, routes, gate_values, weight_in, weight_out):
    groups = lax.axis_size("expert")
    tok_rows, width = tokens.shape
    capacity = min(tok_rows, 2 * tok_rows * routes.shape[1] // groups)
    picks, weighted = slot_matrices(routes, gate_values, groups, capacity)
    step = capacity // CHUNKS
    mixed = None
    for k in range(CHUNKS):
        with jax.named_scope(f"chunk{k}"):
            part = slice(k * step, (k + 1) * step)
            outgoing = jnp.einsum(
                "ect,td->ecd", picks[:, part], tokens, preferred_element_type=jnp.float32
            ).astype(jnp.bfloat16)
            incoming = lax.all_to_all(outgoing, "expert", 0, 0, tiled=True)
            done = expert_rows(incoming.reshape(groups * step, width), weight_in[0], weight_out[0])
            returned = lax.all_to_all(done.reshape(groups, step, width), "expert", 0, 0, tiled=True)
            share = jnp.einsum(
                "ect,ecd->td", weighted[:, part], returned, preferred_element_type=jnp.float32
            )
            mixed = share if mixed is None else mixed + share
    return mixed.astype(jnp.bfloat16)


def solution(mesh):
    in_specs = (
        P(("dp", "expert"), None),
        P(("dp", "expert"), None),
        P(("dp", "expert"), None),
        P("expert", None, None),
        P("expert", None, None),
    )
    out_specs = P(("dp", "expert"), None)
    return jax.shard_map(local, mesh=mesh, in_specs=in_specs, out_specs=out_specs, check_vma=False)
```

```python
import jax
import jax.numpy as jnp
from jax import lax
from jax.sharding import PartitionSpec as P

ROW = 4


def place(index, offset, groups):
    yh, x = index // ROW, index % ROW
    a, b = offset // ROW, offset % ROW
    return ((yh + a) % (groups // ROW)) * ROW + (x + b) % ROW


def back(index, offset, groups):
    yh, x = index // ROW, index % ROW
    a, b = offset // ROW, offset % ROW
    return ((yh - a) % (groups // ROW)) * ROW + (x - b) % ROW


def slot_matrices(routes, gate_values, targets, capacity):
    matched = routes[:, :, None] == targets[None, None, :]
    named = jnp.any(matched, axis=1)
    weight = jnp.sum(jnp.where(matched, gate_values.astype(jnp.float32)[:, :, None], 0.0), axis=1)
    position = jnp.cumsum(named.astype(jnp.int32), axis=0) - 1
    slots = jnp.arange(capacity, dtype=jnp.int32)
    picks = named.T[:, None, :] & (position.T[:, None, :] == slots[None, :, None])
    weighted = jnp.where(picks, weight.T[:, None, :], 0.0)
    return picks.astype(jnp.bfloat16), weighted.astype(jnp.bfloat16)


def local(tokens, routes, gate_values, weight_in, weight_out):
    groups = lax.axis_size("expert")
    tok_rows, width = tokens.shape
    capacity = min(tok_rows, 2 * tok_rows * routes.shape[1] // groups)
    hidden_units = weight_out.shape[1]
    me = lax.axis_index("expert")
    offsets = jnp.arange(groups, dtype=jnp.int32)
    targets = place(me, offsets, groups)
    picks, weighted = slot_matrices(routes, gate_values, targets, capacity)
    outgoing = jnp.einsum(
        "ect,td->ecd", picks, tokens, preferred_element_type=jnp.float32
    ).astype(jnp.bfloat16)
    arrived = [outgoing[0]]
    for o in range(1, groups):
        pairs = [(i, place(i, o, groups)) for i in range(groups)]
        arrived.append(lax.ppermute(outgoing[o], "expert", pairs))
    rows = jnp.stack(arrived).reshape(groups * capacity, width)
    projected = jnp.dot(rows, weight_in[0], preferred_element_type=jnp.float32)
    hidden = (jax.nn.silu(projected[:, :hidden_units]) * projected[:, hidden_units:]).astype(
        jnp.bfloat16
    )
    expert_out = jnp.dot(hidden, weight_out[0], preferred_element_type=jnp.float32)
    expert_out = expert_out.astype(jnp.bfloat16).reshape(groups, capacity, width)
    returned = [expert_out[0]]
    for o in range(1, groups):
        pairs = [(place(i, o, groups), i) for i in range(groups)]
        returned.append(lax.ppermute(expert_out[o], "expert", pairs))
    mixed = jnp.einsum(
        "ect,ecd->td", weighted, jnp.stack(returned), preferred_element_type=jnp.float32
    )
    return mixed.astype(jnp.bfloat16)


def solution(mesh):
    in_specs = (
        P(("dp", "expert"), None),
        P(("dp", "expert"), None),
        P(("dp", "expert"), None),
        P("expert", None, None),
        P("expert", None, None),
    )
    out_specs = P(("dp", "expert"), None)
    return jax.shard_map(local, mesh=mesh, in_specs=in_specs, out_specs=out_specs, check_vma=False)
```

```python
import jax
import jax.numpy as jnp
from jax import lax
from jax.sharding import PartitionSpec as P


def slot_matrices(routes, gate_values, groups, capacity):
    tok_rows = routes.shape[0]
    experts = jnp.arange(groups, dtype=jnp.int32)
    matched = routes[:, :, None] == experts[None, None, :]
    named = jnp.any(matched, axis=1)
    weight = jnp.sum(jnp.where(matched, gate_values.astype(jnp.float32)[:, :, None], 0.0), axis=1)
    position = jnp.cumsum(named.astype(jnp.int32), axis=0) - 1
    slots = jnp.arange(capacity, dtype=jnp.int32)
    hit = named[:, :, None] & (position[:, :, None] == slots[None, None, :])
    weighted = jnp.where(hit, weight[:, :, None], 0.0).astype(jnp.bfloat16)
    picks = hit.astype(jnp.bfloat16).reshape(tok_rows, groups * capacity).T
    return picks, weighted.reshape(tok_rows, groups * capacity)


def local(tokens, routes, gate_values, weight_in, weight_out):
    groups = lax.axis_size("expert")
    tok_rows, width = tokens.shape
    capacity = min(tok_rows, 2 * tok_rows * routes.shape[1] // groups)
    hidden_units = weight_out.shape[1]
    picks, weighted = lax.optimization_barrier(
        slot_matrices(routes, gate_values, groups, capacity)
    )
    outgoing = jnp.dot(picks, tokens, preferred_element_type=jnp.float32).astype(jnp.bfloat16)
    rows = lax.all_to_all(outgoing, "expert", 0, 0, tiled=True)
    projected = jnp.dot(rows, weight_in[0], preferred_element_type=jnp.float32)
    hidden = (jax.nn.silu(projected[:, :hidden_units]) * projected[:, hidden_units:]).astype(
        jnp.bfloat16
    )
    expert_out = jnp.dot(hidden, weight_out[0], preferred_element_type=jnp.float32)
    returned = lax.all_to_all(expert_out.astype(jnp.bfloat16), "expert", 0, 0, tiled=True)
    mixed = jnp.dot(weighted, returned, preferred_element_type=jnp.float32)
    return mixed.astype(jnp.bfloat16)


def solution(mesh):
    in_specs = (
        P(("dp", "expert"), None),
        P(("dp", "expert"), None),
        P(("dp", "expert"), None),
        P("expert", None, None),
        P("expert", None, None),
    )
    out_specs = P(("dp", "expert"), None)
    return jax.shard_map(local, mesh=mesh, in_specs=in_specs, out_specs=out_specs, check_vma=False)
```

```python
import jax
import jax.numpy as jnp
from jax import lax
from jax.sharding import PartitionSpec as P


def slot_matrices(routes, gate_values, groups, capacity):
    tok_rows = routes.shape[0]
    experts = jnp.arange(groups, dtype=jnp.int32)
    matched = routes[:, :, None] == experts[None, None, :]
    named = jnp.any(matched, axis=1)
    weight = jnp.sum(jnp.where(matched, gate_values.astype(jnp.float32)[:, :, None], 0.0), axis=1)
    order = jnp.arange(tok_rows, dtype=jnp.int32)
    earlier = (order[:, None] >= order[None, :]).astype(jnp.bfloat16)
    count = jnp.dot(earlier, named.astype(jnp.bfloat16), preferred_element_type=jnp.float32)
    slots = jnp.arange(capacity, dtype=jnp.float32) + 1.0
    hit = named[:, :, None] & (count[:, :, None] == slots[None, None, :])
    weighted = jnp.where(hit, weight[:, :, None], 0.0).astype(jnp.bfloat16)
    picks = hit.astype(jnp.bfloat16)
    return (picks.reshape(tok_rows, groups * capacity), weighted.reshape(tok_rows, groups * capacity))


def local(tokens, routes, gate_values, weight_in, weight_out):
    groups = lax.axis_size("expert")
    tok_rows, width = tokens.shape
    capacity = min(tok_rows, 2 * tok_rows * routes.shape[1] // groups)
    hidden_units = weight_out.shape[1]
    picks, weighted = lax.optimization_barrier(
        slot_matrices(routes, gate_values, groups, capacity)
    )
    outgoing = lax.dot_general(
        picks, tokens, (((0,), (0,)), ((), ())), preferred_element_type=jnp.float32
    ).astype(jnp.bfloat16)
    rows = lax.all_to_all(outgoing, "expert", 0, 0, tiled=True)
    projected = jnp.dot(rows, weight_in[0], preferred_element_type=jnp.float32)
    hidden = (jax.nn.silu(projected[:, :hidden_units]) * projected[:, hidden_units:]).astype(
        jnp.bfloat16
    )
    expert_out = jnp.dot(hidden, weight_out[0], preferred_element_type=jnp.float32)
    returned = lax.all_to_all(expert_out.astype(jnp.bfloat16), "expert", 0, 0, tiled=True)
    mixed = jnp.dot(weighted, returned, preferred_element_type=jnp.float32)
    return mixed.astype(jnp.bfloat16)


def solution(mesh):
    in_specs = (
        P(("dp", "expert"), None),
        P(("dp", "expert"), None),
        P(("dp", "expert"), None),
        P("expert", None, None),
        P("expert", None, None),
    )
    out_specs = P(("dp", "expert"), None)
    return jax.shard_map(local, mesh=mesh, in_specs=in_specs, out_specs=out_specs, check_vma=False)
```

```python
import jax
import jax.numpy as jnp
from jax import lax
from jax.sharding import PartitionSpec as P


def slot_matrices(routes, gate_values, groups, capacity):
    tok_rows = routes.shape[0]
    column = jnp.arange(groups * capacity, dtype=jnp.int32)[None, :]
    expert_of, slot_of = column // capacity, column % capacity
    first = routes[:, 0:1] == expert_of
    second = routes[:, 1:2] == expert_of
    named = first | second
    order = jnp.arange(tok_rows, dtype=jnp.int32)
    earlier = (order[:, None] >= order[None, :]).astype(jnp.bfloat16)
    count = jnp.dot(earlier, named.astype(jnp.bfloat16), preferred_element_type=jnp.float32)
    hit = named & (count == (slot_of + 1).astype(jnp.float32))
    gates = gate_values.astype(jnp.float32)
    weight = jnp.where(first, gates[:, 0:1], jnp.where(second, gates[:, 1:2], 0.0))
    weighted = jnp.where(hit, weight, 0.0).astype(jnp.bfloat16)
    return hit.astype(jnp.bfloat16), weighted


def local(tokens, routes, gate_values, weight_in, weight_out):
    groups = lax.axis_size("expert")
    tok_rows, width = tokens.shape
    capacity = min(tok_rows, 2 * tok_rows * routes.shape[1] // groups)
    hidden_units = weight_out.shape[1]
    picks, weighted = lax.optimization_barrier(
        slot_matrices(routes, gate_values, groups, capacity)
    )
    outgoing = lax.dot_general(
        picks, tokens, (((0,), (0,)), ((), ())), preferred_element_type=jnp.float32
    ).astype(jnp.bfloat16)
    rows = lax.all_to_all(outgoing, "expert", 0, 0, tiled=True)
    projected = jnp.dot(rows, weight_in[0], preferred_element_type=jnp.float32)
    hidden = (jax.nn.silu(projected[:, :hidden_units]) * projected[:, hidden_units:]).astype(
        jnp.bfloat16
    )
    expert_out = jnp.dot(hidden, weight_out[0], preferred_element_type=jnp.float32)
    returned = lax.all_to_all(expert_out.astype(jnp.bfloat16), "expert", 0, 0, tiled=True)
    mixed = jnp.dot(weighted, returned, preferred_element_type=jnp.float32)
    return mixed.astype(jnp.bfloat16)


def solution(mesh):
    in_specs = (
        P(("dp", "expert"), None),
        P(("dp", "expert"), None),
        P(("dp", "expert"), None),
        P("expert", None, None),
        P("expert", None, None),
    )
    out_specs = P(("dp", "expert"), None)
    return jax.shard_map(local, mesh=mesh, in_specs=in_specs, out_specs=out_specs, check_vma=False)
```

```python
import jax
import jax.numpy as jnp
from jax import lax
from jax.sharding import PartitionSpec as P


def slot_matrices(routes, gate_values, groups, capacity):
    tok_rows = routes.shape[0]
    column = jnp.arange(groups * capacity, dtype=jnp.int32)[None, :]
    expert_of, slot_of = column // capacity, column % capacity
    first = routes[:, 0:1] == expert_of
    second = routes[:, 1:2] == expert_of
    named = first | second
    order = jnp.arange(tok_rows, dtype=jnp.int32)
    earlier = (order[:, None] >= order[None, :]).astype(jnp.bfloat16)
    count = jnp.dot(earlier, named.astype(jnp.bfloat16), preferred_element_type=jnp.float32)
    hit = named & (count == (slot_of + 1).astype(jnp.float32))
    gates = gate_values.astype(jnp.float32)
    weight = jnp.where(first, gates[:, 0:1], jnp.where(second, gates[:, 1:2], 0.0))
    weighted = jnp.where(hit, weight, 0.0).astype(jnp.bfloat16)
    return hit.astype(jnp.bfloat16), weighted


def local(tokens, routes, gate_values, weight_in, weight_out):
    groups = lax.axis_size("expert")
    tok_rows, width = tokens.shape
    capacity = min(tok_rows, 2 * tok_rows * routes.shape[1] // groups)
    hidden_units = weight_out.shape[1]
    picks, weighted = lax.optimization_barrier(
        slot_matrices(routes, gate_values, groups, capacity)
    )
    outgoing = lax.dot_general(
        picks, tokens, (((0,), (0,)), ((), ())), preferred_element_type=jnp.float32
    ).astype(jnp.bfloat16)
    rows = lax.all_to_all(outgoing, "expert", 0, 0, tiled=True)
    projected = jnp.dot(rows, weight_in[0], preferred_element_type=jnp.float32)
    hidden = (jax.nn.silu(projected[:, :hidden_units]) * projected[:, hidden_units:]).astype(
        jnp.bfloat16
    )
    half = width // 2
    parts = []
    for k in range(2):
        with jax.named_scope(f"cols{k}"):
            cols = slice(k * half, (k + 1) * half)
            expert_out = jnp.dot(hidden, weight_out[0][:, cols], preferred_element_type=jnp.float32)
            returned = lax.all_to_all(expert_out.astype(jnp.bfloat16), "expert", 0, 0, tiled=True)
            parts.append(jnp.dot(weighted, returned, preferred_element_type=jnp.float32).astype(jnp.bfloat16))
    return jnp.concatenate(parts, axis=1)


def solution(mesh):
    in_specs = (
        P(("dp", "expert"), None),
        P(("dp", "expert"), None),
        P(("dp", "expert"), None),
        P("expert", None, None),
        P("expert", None, None),
    )
    out_specs = P(("dp", "expert"), None)
    return jax.shard_map(local, mesh=mesh, in_specs=in_specs, out_specs=out_specs, check_vma=False)
```

```python
import jax
import jax.numpy as jnp
from jax import lax
from jax.sharding import PartitionSpec as P


def slot_matrices(routes, gate_values, groups, capacity):
    tok_rows = routes.shape[0]
    column = jnp.arange(groups * capacity, dtype=jnp.int32)[None, :]
    expert_of, slot_of = column // capacity, column % capacity
    first = routes[:, 0:1] == expert_of
    second = routes[:, 1:2] == expert_of
    named = first | second
    order = jnp.arange(tok_rows, dtype=jnp.int32)
    earlier = (order[:, None] >= order[None, :]).astype(jnp.bfloat16)
    count = jnp.dot(earlier, named.astype(jnp.bfloat16), preferred_element_type=jnp.float32)
    hit = named & (count == (slot_of + 1).astype(jnp.float32))
    gates = gate_values.astype(jnp.float32)
    weight = jnp.where(first, gates[:, 0:1], jnp.where(second, gates[:, 1:2], 0.0))
    weighted = jnp.where(hit, weight, 0.0).astype(jnp.bfloat16)
    return hit.astype(jnp.bfloat16), weighted


def local(tokens, routes, gate_values, weight_in, weight_out):
    groups = lax.axis_size("expert")
    tok_rows, width = tokens.shape
    capacity = min(tok_rows, 2 * tok_rows * routes.shape[1] // groups)
    hidden_units = weight_out.shape[1]
    picks, weighted = lax.optimization_barrier(
        slot_matrices(routes, gate_values, groups, capacity)
    )
    outgoing = lax.dot_general(
        picks, tokens, (((0,), (0,)), ((), ())), preferred_element_type=jnp.float32
    ).astype(jnp.bfloat16)
    rows = lax.all_to_all(outgoing, "expert", 0, 0, tiled=True)
    gate_part = jnp.dot(rows, weight_in[0][:, :hidden_units], preferred_element_type=jnp.float32)
    up_part = jnp.dot(rows, weight_in[0][:, hidden_units:], preferred_element_type=jnp.float32)
    hidden = (jax.nn.silu(gate_part) * up_part).astype(jnp.bfloat16)
    expert_out = jnp.dot(hidden, weight_out[0], preferred_element_type=jnp.float32)
    returned = lax.all_to_all(expert_out.astype(jnp.bfloat16), "expert", 0, 0, tiled=True)
    mixed = jnp.dot(weighted, returned, preferred_element_type=jnp.float32)
    return mixed.astype(jnp.bfloat16)


def solution(mesh):
    in_specs = (
        P(("dp", "expert"), None),
        P(("dp", "expert"), None),
        P(("dp", "expert"), None),
        P("expert", None, None),
        P("expert", None, None),
    )
    out_specs = P(("dp", "expert"), None)
    return jax.shard_map(local, mesh=mesh, in_specs=in_specs, out_specs=out_specs, check_vma=False)
```

```python
import jax
import jax.numpy as jnp
from jax import lax
from jax.sharding import PartitionSpec as P


def slot_matrices(routes, gate_values, groups, capacity):
    tok_rows = routes.shape[0]
    row = jnp.arange(groups * capacity, dtype=jnp.int32)[:, None]
    expert_of, slot_of = row // capacity, row % capacity
    named_by = routes.T
    first = named_by[0:1, :] == expert_of
    second = named_by[1:2, :] == expert_of
    named = first | second
    order = jnp.arange(tok_rows, dtype=jnp.int32)
    later = (order[:, None] <= order[None, :]).astype(jnp.bfloat16)
    count = jnp.dot(named.astype(jnp.bfloat16), later, preferred_element_type=jnp.float32)
    hit = named & (count == (slot_of + 1).astype(jnp.float32))
    gates = gate_values.astype(jnp.float32).T
    weight = jnp.where(first, gates[0:1, :], jnp.where(second, gates[1:2, :], 0.0))
    weighted = jnp.where(hit, weight, 0.0).astype(jnp.bfloat16)
    return hit.astype(jnp.bfloat16), weighted


def local(tokens, routes, gate_values, weight_in, weight_out):
    groups = lax.axis_size("expert")
    tok_rows, width = tokens.shape
    capacity = min(tok_rows, 2 * tok_rows * routes.shape[1] // groups)
    hidden_units = weight_out.shape[1]
    picks, weighted = lax.optimization_barrier(
        slot_matrices(routes, gate_values, groups, capacity)
    )
    outgoing = jnp.dot(picks, tokens, preferred_element_type=jnp.float32).astype(jnp.bfloat16)
    rows = lax.all_to_all(outgoing, "expert", 0, 0, tiled=True)
    projected = jnp.dot(rows, weight_in[0], preferred_element_type=jnp.float32)
    hidden = (jax.nn.silu(projected[:, :hidden_units]) * projected[:, hidden_units:]).astype(
        jnp.bfloat16
    )
    expert_out = jnp.dot(hidden, weight_out[0], preferred_element_type=jnp.float32)
    returned = lax.all_to_all(expert_out.astype(jnp.bfloat16), "expert", 0, 0, tiled=True)
    mixed = lax.dot_general(
        weighted, returned, (((0,), (0,)), ((), ())), preferred_element_type=jnp.float32
    )
    return mixed.astype(jnp.bfloat16)


def solution(mesh):
    in_specs = (
        P(("dp", "expert"), None),
        P(("dp", "expert"), None),
        P(("dp", "expert"), None),
        P("expert", None, None),
        P("expert", None, None),
    )
    out_specs = P(("dp", "expert"), None)
    return jax.shard_map(local, mesh=mesh, in_specs=in_specs, out_specs=out_specs, check_vma=False)
```

```python
import functools

import jax
import jax.numpy as jnp
from jax import lax
from jax.experimental import pallas as pl
from jax.experimental.pallas import tpu as pltpu
from jax.sharding import PartitionSpec as P

INTERPRET = False


def dispatch_kernel(capacity, block, routes_ref, gates_ref, tokens_ref, out_ref, weighted_ref):
    slots, tok_rows = weighted_ref.shape
    width = tokens_ref.shape[1]
    shift = capacity.bit_length() - 1
    row = lax.broadcasted_iota(jnp.int32, (slots, tok_rows), 0)
    expert_of = lax.shift_right_logical(row, shift)
    slot_of = lax.bitwise_and(row, capacity - 1)
    routes = routes_ref[...]
    gates = gates_ref[...].astype(jnp.float32)
    first = routes[0:1, :] == expert_of
    second = routes[1:2, :] == expert_of
    named = jnp.where(first | second, 1.0, 0.0).astype(jnp.bfloat16)
    above = lax.broadcasted_iota(jnp.int32, (tok_rows, tok_rows), 0)
    below = lax.broadcasted_iota(jnp.int32, (tok_rows, tok_rows), 1)
    later = jnp.where(above <= below, 1.0, 0.0).astype(jnp.bfloat16)
    count = jnp.dot(named, later, preferred_element_type=jnp.float32)
    hit = (first | second) & (count == (slot_of + 1).astype(jnp.float32))
    weight = jnp.where(first, gates[0:1, :], jnp.where(second, gates[1:2, :], 0.0))
    weighted_ref[...] = jnp.where(hit, weight, 0.0).astype(jnp.bfloat16)
    picks = jnp.where(hit, 1.0, 0.0).astype(jnp.bfloat16)
    for k in range(width // block):
        cols = slice(k * block, (k + 1) * block)
        out_ref[:, cols] = jnp.dot(
            picks, tokens_ref[:, cols], preferred_element_type=jnp.float32
        ).astype(out_ref.dtype)


def dispatch(routes, gate_values, tokens, groups, capacity):
    tok_rows, width = tokens.shape
    slots = groups * capacity
    return pl.pallas_call(
        functools.partial(dispatch_kernel, capacity, 512),
        out_shape=(
            jax.ShapeDtypeStruct((slots, width), tokens.dtype),
            jax.ShapeDtypeStruct((slots, tok_rows), jnp.bfloat16),
        ),
        in_specs=[pl.BlockSpec(memory_space=pltpu.VMEM)] * 3,
        out_specs=(pl.BlockSpec(memory_space=pltpu.VMEM), pl.BlockSpec(memory_space=pltpu.VMEM)),
        compiler_params=pltpu.CompilerParams(vmem_limit_bytes=48 * 1024 * 1024),
        interpret=INTERPRET,
    )(routes.T, gate_values.T, tokens)


def local(tokens, routes, gate_values, weight_in, weight_out):
    groups = lax.axis_size("expert")
    tok_rows, width = tokens.shape
    capacity = min(tok_rows, 2 * tok_rows * routes.shape[1] // groups)
    assert capacity & (capacity - 1) == 0
    hidden_units = weight_out.shape[1]
    outgoing, weighted = dispatch(routes, gate_values, tokens, groups, capacity)
    rows = lax.all_to_all(outgoing, "expert", 0, 0, tiled=True)
    projected = jnp.dot(rows, weight_in[0], preferred_element_type=jnp.float32)
    hidden = (jax.nn.silu(projected[:, :hidden_units]) * projected[:, hidden_units:]).astype(
        jnp.bfloat16
    )
    expert_out = jnp.dot(hidden, weight_out[0], preferred_element_type=jnp.float32)
    returned = lax.all_to_all(expert_out.astype(jnp.bfloat16), "expert", 0, 0, tiled=True)
    mixed = lax.dot_general(
        weighted, returned, (((0,), (0,)), ((), ())), preferred_element_type=jnp.float32
    )
    return mixed.astype(jnp.bfloat16)


def solution(mesh):
    in_specs = (
        P(("dp", "expert"), None),
        P(("dp", "expert"), None),
        P(("dp", "expert"), None),
        P("expert", None, None),
        P("expert", None, None),
    )
    out_specs = P(("dp", "expert"), None)
    return jax.shard_map(local, mesh=mesh, in_specs=in_specs, out_specs=out_specs, check_vma=False)
```

```python
import jax
import jax.numpy as jnp
from jax import lax
from jax.sharding import PartitionSpec as P


def slot_matrices(routes, gate_values, groups, capacity):
    tok_rows = routes.shape[0]
    row = jnp.arange(groups * capacity, dtype=jnp.int32)[:, None]
    expert_of, slot_of = row // capacity, row % capacity
    named_by = routes.T
    first = named_by[0:1, :] == expert_of
    second = named_by[1:2, :] == expert_of
    named = first | second
    order = jnp.arange(tok_rows, dtype=jnp.int32)
    later = (order[:, None] <= order[None, :]).astype(jnp.bfloat16)
    count = jnp.dot(named.astype(jnp.bfloat16), later, preferred_element_type=jnp.float32)
    hit = named & (count == (slot_of + 1).astype(jnp.float32))
    gates = gate_values.astype(jnp.float32).T
    weight = jnp.where(first, gates[0:1, :], jnp.where(second, gates[1:2, :], 0.0))
    weighted = jnp.where(hit, weight, 0.0).astype(jnp.bfloat16)
    return hit.astype(jnp.bfloat16), weighted


def local(tokens, routes, gate_values, weight_in, weight_out):
    groups = lax.axis_size("expert")
    tok_rows, width = tokens.shape
    capacity = min(tok_rows, 2 * tok_rows * routes.shape[1] // groups)
    hidden_units = weight_out.shape[1]
    picks, weighted = slot_matrices(routes, gate_values, groups, capacity)
    outgoing = jnp.dot(picks, tokens, preferred_element_type=jnp.float32).astype(jnp.bfloat16)
    rows = lax.all_to_all(outgoing, "expert", 0, 0, tiled=True)
    projected = jnp.dot(rows, weight_in[0], preferred_element_type=jnp.float32)
    hidden = (jax.nn.silu(projected[:, :hidden_units]) * projected[:, hidden_units:]).astype(
        jnp.bfloat16
    )
    expert_out = jnp.dot(hidden, weight_out[0], preferred_element_type=jnp.float32)
    returned = lax.all_to_all(expert_out.astype(jnp.bfloat16), "expert", 0, 0, tiled=True)
    mixed = lax.dot_general(
        weighted, returned, (((0,), (0,)), ((), ())), preferred_element_type=jnp.float32
    )
    return mixed.astype(jnp.bfloat16)


def solution(mesh):
    in_specs = (
        P(("dp", "expert"), None),
        P(("dp", "expert"), None),
        P(("dp", "expert"), None),
        P("expert", None, None),
        P("expert", None, None),
    )
    out_specs = P(("dp", "expert"), None)
    return jax.shard_map(local, mesh=mesh, in_specs=in_specs, out_specs=out_specs, check_vma=False)
```
